32 devices in a mesh: seq: 16 (over z, x, core), batch: 2 (over y).
Axes of the slice: x: 2, y: 2, z: 4, core: 2. Of those that a mesh axis runs over, the one named last changes fastest.
Arguments:
- activations: bfloat16 [2, 8192, 1536], P('batch', 'seq'), may hold values from -60 to 60
- cotangent: bfloat16 [2, 8192, 1536], P('batch', 'seq'), may hold values from -6 to 6
- contig_lengths: int32 [2, 4], P('batch'), may hold values from 1 to 4096, 8192 in all within a row
- gain_input: float32 [1536], replicated, may hold values from 0.1 to 1.9
- tap_weights: bfloat16 [3, 1536, 768], replicated, may hold values from -0.09375 to 0.09375
- gain_middle: float32 [768], replicated, may hold values from 0.1 to 1.9
- point_weights: bfloat16 [768, 1536], replicated, may hold values from -0.21875 to 0.21875
Outputs:
- block_output: bfloat16 [2, 8192, 1536], P('batch', 'seq')
- input_grad: bfloat16 [2, 8192, 1536], P('batch', 'seq')
- gain_input_grad: float32 [1536], replicated
- gain_middle_grad: float32 [768], replicated
The draws below stay inside these ranges and needn't reach their ends.
Inputs may be any that keep to these rules, and one draw needn't show every extreme that they name: `contig_lengths`: row w lists in order the lengths of the 4 contigs packed into window w; they sum to 8192.
All inputs are finite; a program needn't handle non-finite values.
Results may differ from the reference program's by a relative error of at most 0.0065.
Values may be sent and summed in bfloat16 or wider, within the bound.
No kernel may reach another device: no remote copies, remote signals or barrier semaphores. Data moves between devices by JAX's collectives and lax.ppermute only.
A program may use at most 64 MiB of HBM per device.

```python
import math
import jax
import jax.numpy as jnp
import numpy as np
from jax import lax

C = 1536
F = 768
ROWS_DEV = 512
SPAN = 2
NCONTIG = 4
LENGTH = 8192
WINDOWS = 2


def draw_activations(key, part):
    full_shape = (WINDOWS, LENGTH, C)
    key_values, key_rows, key_columns = jax.random.split(key, 3)
    lowest = math.log(0.3)
    highest = math.log(3.0)
    row_scale = jnp.exp(jax.random.uniform(key_rows, (WINDOWS, LENGTH, 1), jnp.float32, lowest, highest))
    column_scale = jnp.exp(jax.random.uniform(key_columns, (1, 1, C), jnp.float32, lowest, highest))
    values = jnp.clip(jax.random.normal(key_values, full_shape, jnp.float32), -6.0, 6.0)
    return (values * row_scale * column_scale).astype(jnp.bfloat16)


def shard_levels(own_key, extent, cuts, smallest, high):
    loudness = 1.0
    for axis_at, blocks in cuts:
        draws = jax.random.uniform(jax.random.fold_in(jax.random.fold_in(own_key, 6), axis_at), (blocks,), jnp.float32, smallest / len(cuts), high / len(cuts))
        loudness = loudness * jnp.repeat(jnp.exp(draws), extent[axis_at] // blocks).reshape((-1,) + (1,) * (len(extent) - 1 - axis_at))
    return loudness


def split_up(amount, total, most, slope):
    loads = [(1 << 20) // math.isqrt(rank ** slope) + 1 for rank in range(2, amount + 1)]
    spare, holding = total - most - (amount - 1), [1] * (amount - 1)
    while spare > 0:
        movable = [i for i in range(amount - 1) if holding[i] < most]
        whole, budget = sum([loads[i] for i in movable]), spare
        for i in movable:
            more = min(most - holding[i], max(1, budget * loads[i] // whole), spare)
            holding[i] = holding[i] + more
            spare = spare - more
    return np.array([most] + holding)


def uneven(key, number_of, total, bound, lean):
    if number_of == 2:
        one = jax.random.randint(key, (), max(1, total - bound), min(bound, total - 1) + 1)
        return jnp.stack([one, total - one])
    sizes = jnp.asarray(split_up(number_of, total, bound, lean), jnp.int32)
    couples = (number_of - 1) // 2
    source_of, receiver = sizes[1:1 + 2 * couples:2], sizes[2:2 + 2 * couples:2]
    room = jnp.minimum(source_of - 1, bound - receiver)
    moved = jax.random.randint(jax.random.fold_in(key, 1), (couples,), 0, 1 << 20) % (room + 1)
    sizes = sizes.at[1:1 + 2 * couples:2].set(source_of - moved).at[2:2 + 2 * couples:2].set(receiver + moved)
    return sizes[jax.random.permutation(jax.random.fold_in(key, 2), number_of)]


def centred(rng, shape, scale, limit, shards=(), kind=jnp.bfloat16):
    gain = shard_levels(rng, shape, shards, -0.22, 0.18) if shards else 1.0
    values = jax.random.normal(rng, shape, jnp.float32) * scale * gain
    return jnp.minimum(jnp.maximum(values, -limit), limit).astype(kind)


def setup_inputs(seed: int = 0) -> dict:
    key_list = jax.random.split(jax.random.key(seed), 8)
    return {
        "activations": draw_activations(jax.random.fold_in(key_list[7], 71), 0),
        "cotangent": centred(key_list[1], (WINDOWS, LENGTH, C), 1.0, 6.0, ((0, 2), (1, 16))),
        "contig_lengths": jax.vmap(lambda own: uneven(own, NCONTIG, LENGTH, LENGTH // 2, 2))(jax.random.split(key_list[2], WINDOWS)).reshape((WINDOWS, NCONTIG)).astype(jnp.int32),
        "gain_input": jnp.clip(1.0 + 0.18 * jax.random.normal(key_list[3], (C,), jnp.float32), 0.1, 1.9),
        "tap_weights": centred(key_list[4], (3, C, F), (3 * C) ** -0.5, 0.09375),
        "gain_middle": jnp.clip(1.0 + 0.18 * jax.random.normal(key_list[5], (F,), jnp.float32), 0.1, 1.9),
        "point_weights": centred(key_list[6], (F, C), F ** -0.5, 0.21875),
    }


epsilon = 1e-06

def norm_activate(values, scales):
    mean_square = lax.optimization_barrier(jnp.mean(values * values, axis=-1, keepdims=True))
    return jax.nn.gelu(values * lax.rsqrt(mean_square + epsilon) * scales, approximate=True)

def contig_owner(lengths, positions):
    bounds = jnp.cumsum(lengths).astype(jnp.int32)
    return lax.optimization_barrier(jnp.sum((positions[:, None] >= bounds[None, :]).astype(jnp.int32), axis=1)).astype(jnp.int32)

def shifted(values, offset):
    padding = jnp.zeros((abs(offset),) + values.shape[1:], values.dtype)
    if offset > 0:
        return jnp.concatenate([values[offset:], padding], axis=0)
    return jnp.concatenate([padding, values[:offset]], axis=0)

def reference(activations, cotangent, contig_lengths, gain_input, tap_weights, gain_middle, point_weights):
    tap_reach = SPAN * ROWS_DEV
    positions = jnp.arange(LENGTH, dtype=jnp.int32)
    tap_before = tap_weights[0]
    tap_center = tap_weights[1]
    tap_after = tap_weights[2]

    def window(inputs):
        signal, upstream, lengths = inputs
        owners = contig_owner(lengths, positions)
        before_valid = ((positions >= tap_reach) & (shifted(owners, -tap_reach) == owners)).astype(jnp.float32)[:, None]
        after_valid = ((positions < LENGTH - tap_reach) & (shifted(owners, tap_reach) == owners)).astype(jnp.float32)[:, None]
        normed, input_vjp = jax.vjp(norm_activate, signal.astype(jnp.float32), gain_input)
        hidden = normed.astype(jnp.bfloat16)
        combined = jnp.dot(hidden, tap_center, preferred_element_type=jnp.float32)
        combined = combined + before_valid * jnp.dot(shifted(hidden, -tap_reach), tap_before, preferred_element_type=jnp.float32)
        combined = combined + after_valid * jnp.dot(shifted(hidden, tap_reach), tap_after, preferred_element_type=jnp.float32)
        middle_f, middle_vjp = jax.vjp(norm_activate, combined, gain_middle)
        middle = middle_f.astype(jnp.bfloat16)
        output = (signal.astype(jnp.float32) + jnp.dot(middle, point_weights, preferred_element_type=jnp.float32)).astype(jnp.bfloat16)
        grad_middle = jnp.dot(upstream, point_weights.T, preferred_element_type=jnp.float32)
        grad_combined_f, middle_terms = middle_vjp(grad_middle)
        grad_combined = grad_combined_f.astype(jnp.bfloat16)
        grad_hidden = jnp.dot(grad_combined, tap_center.T, preferred_element_type=jnp.float32)
        grad_hidden = grad_hidden + before_valid * jnp.dot(shifted(grad_combined, -tap_reach), tap_after.T, preferred_element_type=jnp.float32)
        grad_hidden = grad_hidden + after_valid * jnp.dot(shifted(grad_combined, tap_reach), tap_before.T, preferred_element_type=jnp.float32)
        grad_signal, input_terms = input_vjp(grad_hidden)
        grad_output = (upstream.astype(jnp.float32) + grad_signal).astype(jnp.bfloat16)
        return (output, grad_output, input_terms, middle_terms)
    outputs, grads, input_terms, middle_terms = lax.map(window, (activations, cotangent, contig_lengths))
    factor = 1.0 / (WINDOWS * LENGTH) ** 0.5
    return (outputs, grads, lax.optimization_barrier(jnp.sum(input_terms, axis=0)) * factor, lax.optimization_barrier(jnp.sum(middle_terms, axis=0)) * factor)
```

```python
import math

import jax
import jax.numpy as jnp
from jax import lax
from jax.sharding import PartitionSpec as P

SPAN = 2
REDUCE = "butterfly"


epsilon = 1e-06


def shifted(x, axis, by):
    peers = lax.axis_size(axis)
    pairs = [(i, i + by) for i in range(peers) if 0 <= i + by < peers]
    return lax.ppermute(x, axis, pairs)


def norm_activate(values, scales):
    mean_square = jnp.mean(values * values, axis=-1, keepdims=True)
    return jax.nn.gelu(values * lax.rsqrt(mean_square + epsilon) * scales, approximate=True)


def contig_owner(lengths, positions):
    bounds = jnp.cumsum(lengths)
    return jnp.sum((positions[:, None] >= bounds[None, :]).astype(jnp.int32), axis=1)


def reduce_all(x):
    if REDUCE == "psum_flat":
        return lax.psum(x, ("seq", "batch"))
    if REDUCE == "psum_nested":
        return lax.psum(lax.psum(x, "seq"), "batch")
    if REDUCE == "scatter_gather":
        part = lax.psum_scatter(x, ("seq", "batch"), scatter_dimension=0, tiled=True)
        return lax.all_gather(part, ("seq", "batch"), axis=0, tiled=True)
    if REDUCE == "gather_sum":
        return jnp.sum(lax.all_gather(x, ("seq", "batch"), axis=0), axis=0)
    if REDUCE == "butterfly":
        for axis in ("seq", "batch"):
            size = lax.axis_size(axis)
            step = 1
            while step < size:
                pairs = [(i, i ^ step) for i in range(size)]
                x = x + lax.ppermute(x, axis, pairs)
                step *= 2
        return x
    raise ValueError(REDUCE)


def body(
    activations, cotangent, contig_lengths, gain_input, tap_weights, gain_middle, point_weights
):
    signal = activations[0]
    upstream = cotangent[0]
    lengths = contig_lengths[0]
    shard_rows = signal.shape[0]
    seq_count = lax.axis_size("seq")
    tap_reach = SPAN * shard_rows
    total_length = shard_rows * seq_count
    positions = lax.axis_index("seq") * shard_rows + jnp.arange(shard_rows, dtype=jnp.int32)
    owners = contig_owner(lengths, positions)
    before_valid = (
        (positions >= tap_reach) & (contig_owner(lengths, positions - tap_reach) == owners)
    ).astype(jnp.float32)[:, None]
    after_valid = (
        (positions < total_length - tap_reach)
        & (contig_owner(lengths, positions + tap_reach) == owners)
    ).astype(jnp.float32)[:, None]
    tap_before = tap_weights[0]
    tap_center = tap_weights[1]
    tap_after = tap_weights[2]
    normed, input_vjp = jax.vjp(norm_activate, signal.astype(jnp.float32), gain_input)
    hidden = normed.astype(jnp.bfloat16)
    sent_before = jnp.dot(hidden, tap_before, preferred_element_type=jnp.float32)
    sent_after = jnp.dot(hidden, tap_after, preferred_element_type=jnp.float32)
    product_before = shifted(sent_before.astype(jnp.bfloat16), "seq", SPAN)
    product_after = shifted(sent_after.astype(jnp.bfloat16), "seq", -SPAN)
    combined = jnp.dot(hidden, tap_center, preferred_element_type=jnp.float32)
    grad_middle = jnp.dot(upstream, point_weights.T, preferred_element_type=jnp.float32)
    combined = combined + before_valid * product_before.astype(jnp.float32)
    combined = combined + after_valid * product_after.astype(jnp.float32)
    middle_f, middle_vjp = jax.vjp(norm_activate, combined, gain_middle)
    middle = middle_f.astype(jnp.bfloat16)
    grad_combined_f, middle_terms = middle_vjp(grad_middle)
    grad_combined = grad_combined_f.astype(jnp.bfloat16)
    combined_before = shifted(grad_combined, "seq", SPAN)
    combined_after = shifted(grad_combined, "seq", -SPAN)
    output = (
        signal.astype(jnp.float32)
        + jnp.dot(middle, point_weights, preferred_element_type=jnp.float32)
    ).astype(jnp.bfloat16)
    grad_hidden = jnp.dot(grad_combined, tap_center.T, preferred_element_type=jnp.float32)
    grad_hidden = grad_hidden + before_valid * jnp.dot(
        combined_before, tap_after.T, preferred_element_type=jnp.float32
    )
    grad_hidden = grad_hidden + after_valid * jnp.dot(
        combined_after, tap_before.T, preferred_element_type=jnp.float32
    )
    grad_signal, input_terms = input_vjp(grad_hidden)
    grad_output = (upstream.astype(jnp.float32) + grad_signal).astype(jnp.bfloat16)
    terms = jnp.concatenate([input_terms, middle_terms])
    summed = reduce_all(terms)
    factor = 1.0 / math.sqrt(lax.axis_size("batch") * seq_count * shard_rows)
    channels = input_terms.shape[0]
    return (
        output[None],
        grad_output[None],
        summed[:channels] * factor,
        summed[channels:] * factor,
    )


def solution(mesh):
    placed = (
        P("batch", "seq", None),
        P("batch", "seq", None),
        P("batch", None),
        P(),
        P(),
        P(),
        P(),
    )
    return jax.shard_map(
        body,
        mesh=mesh,
        in_specs=placed,
        out_specs=(P("batch", "seq", None), P("batch", "seq", None), P(), P()),
        check_vma=False,
    )
```

```python
import math

import jax
import jax.numpy as jnp
from jax import lax
from jax.sharding import PartitionSpec as P

SPAN = 2
CHUNKS = 2
RADIX = 4


epsilon = 1e-06


def shifted(x, axis, by):
    peers = lax.axis_size(axis)
    pairs = [(i, i + by) for i in range(peers) if 0 <= i + by < peers]
    return lax.ppermute(x, axis, pairs)


def norm_activate(values, scales):
    mean_square = jnp.mean(values * values, axis=-1, keepdims=True)
    return jax.nn.gelu(values * lax.rsqrt(mean_square + epsilon) * scales, approximate=True)


def contig_owner(lengths, positions):
    bounds = jnp.cumsum(lengths)
    return jnp.sum((positions[:, None] >= bounds[None, :]).astype(jnp.int32), axis=1)


def group_sum(x, axis, stride, radix):
    size = lax.axis_size(axis)
    parts = [x]
    for step in range(1, radix):
        pairs = [(i, i ^ (step * stride)) for i in range(size)]
        parts.append(lax.ppermute(x, axis, pairs))
    while len(parts) > 1:
        parts = [parts[k] + parts[k + 1] for k in range(0, len(parts), 2)]
    return parts[0]


def reduce_all(x):
    axes = ("seq", "batch")
    sizes = [lax.axis_size(a) for a in axes]
    if any(s & (s - 1) for s in sizes):
        return lax.psum(x, axes)
    for axis, size in zip(axes, sizes):
        stride = 1
        while stride < size:
            radix = min(RADIX, size // stride)
            x = group_sum(x, axis, stride, radix)
            stride *= radix
    return x


def body(
    activations, cotangent, contig_lengths, gain_input, tap_weights, gain_middle, point_weights
):
    lengths = contig_lengths[0]
    shard_rows = activations.shape[1]
    seq_count = lax.axis_size("seq")
    tap_reach = SPAN * shard_rows
    total_length = shard_rows * seq_count
    tap_before = tap_weights[0]
    tap_center = tap_weights[1]
    tap_after = tap_weights[2]
    rows = shard_rows // CHUNKS
    first_row = lax.axis_index("seq") * shard_rows

    chunks = []
    for c in range(CHUNKS):
        signal = activations[0, c * rows:(c + 1) * rows]
        upstream = cotangent[0, c * rows:(c + 1) * rows]
        positions = first_row + c * rows + jnp.arange(rows, dtype=jnp.int32)
        owners = contig_owner(lengths, positions)
        before_valid = (
            (positions >= tap_reach) & (contig_owner(lengths, positions - tap_reach) == owners)
        ).astype(jnp.float32)[:, None]
        after_valid = (
            (positions < total_length - tap_reach)
            & (contig_owner(lengths, positions + tap_reach) == owners)
        ).astype(jnp.float32)[:, None]
        normed, input_vjp = jax.vjp(norm_activate, signal.astype(jnp.float32), gain_input)
        hidden = normed.astype(jnp.bfloat16)
        sent_before = jnp.dot(hidden, tap_before, preferred_element_type=jnp.float32)
        sent_after = jnp.dot(hidden, tap_after, preferred_element_type=jnp.float32)
        chunks.append(dict(
            signal=signal, upstream=upstream, before_valid=before_valid,
            after_valid=after_valid, hidden=hidden, input_vjp=input_vjp,
            product_before=shifted(sent_before.astype(jnp.bfloat16), "seq", SPAN),
            product_after=shifted(sent_after.astype(jnp.bfloat16), "seq", -SPAN),
        ))
    for ch in chunks:
        combined = jnp.dot(ch["hidden"], tap_center, preferred_element_type=jnp.float32)
        grad_middle = jnp.dot(ch["upstream"], point_weights.T, preferred_element_type=jnp.float32)
        combined = combined + ch["before_valid"] * ch["product_before"].astype(jnp.float32)
        combined = combined + ch["after_valid"] * ch["product_after"].astype(jnp.float32)
        middle_f, middle_vjp = jax.vjp(norm_activate, combined, gain_middle)
        ch["middle"] = middle_f.astype(jnp.bfloat16)
        grad_combined_f, ch["middle_terms"] = middle_vjp(grad_middle)
        grad_combined = grad_combined_f.astype(jnp.bfloat16)
        ch["grad_combined"] = grad_combined
        ch["combined_before"] = shifted(grad_combined, "seq", SPAN)
        ch["combined_after"] = shifted(grad_combined, "seq", -SPAN)
    outputs, grads = [], []
    input_terms, middle_terms = None, None
    for ch in chunks:
        outputs.append((
            ch["signal"].astype(jnp.float32)
            + jnp.dot(ch["middle"], point_weights, preferred_element_type=jnp.float32)
        ).astype(jnp.bfloat16))
        grad_hidden = jnp.dot(ch["grad_combined"], tap_center.T, preferred_element_type=jnp.float32)
        grad_hidden = grad_hidden + ch["before_valid"] * jnp.dot(
            ch["combined_before"], tap_after.T, preferred_element_type=jnp.float32
        )
        grad_hidden = grad_hidden + ch["after_valid"] * jnp.dot(
            ch["combined_after"], tap_before.T, preferred_element_type=jnp.float32
        )
        grad_signal, terms = ch["input_vjp"](grad_hidden)
        grads.append((ch["upstream"].astype(jnp.float32) + grad_signal).astype(jnp.bfloat16))
        input_terms = terms if input_terms is None else input_terms + terms
        middle_terms = ch["middle_terms"] if middle_terms is None else middle_terms + ch["middle_terms"]
    summed = reduce_all(jnp.concatenate([input_terms, middle_terms]))
    factor = 1.0 / math.sqrt(lax.axis_size("batch") * seq_count * shard_rows)
    channels = input_terms.shape[0]
    return (
        jnp.concatenate(outputs)[None],
        jnp.concatenate(grads)[None],
        summed[:channels] * factor,
        summed[channels:] * factor,
    )


def solution(mesh):
    placed = (
        P("batch", "seq", None),
        P("batch", "seq", None),
        P("batch", None),
        P(),
        P(),
        P(),
        P(),
    )
    return jax.shard_map(
        body,
        mesh=mesh,
        in_specs=placed,
        out_specs=(P("batch", "seq", None), P("batch", "seq", None), P(), P()),
        check_vma=False,
    )
```

```python
import math

import jax
import jax.numpy as jnp
from jax import lax
from jax.sharding import PartitionSpec as P

SPAN = 2
CHUNKS = (1, 1)
AXES = ("seq", "batch")
RADIX = 4
EARLY = True
LATE_OUTPUT = True


epsilon = 1e-06


def shifted(x, axis, by):
    peers = lax.axis_size(axis)
    pairs = [(i, i + by) for i in range(peers) if 0 <= i + by < peers]
    return lax.ppermute(x, axis, pairs)


def norm_activate(values, scales):
    mean_square = jnp.mean(values * values, axis=-1, keepdims=True)
    return jax.nn.gelu(values * lax.rsqrt(mean_square + epsilon) * scales, approximate=True)


def contig_owner(lengths, positions):
    bounds = jnp.cumsum(lengths)
    return jnp.sum((positions[:, None] >= bounds[None, :]).astype(jnp.int32), axis=1)


def group_sum(x, axis, stride, radix):
    size = lax.axis_size(axis)
    parts = [x]
    for step in range(1, radix):
        pairs = [(i, i ^ (step * stride)) for i in range(size)]
        parts.append(lax.ppermute(x, axis, pairs))
    while len(parts) > 1:
        parts = [parts[k] + parts[k + 1] for k in range(0, len(parts), 2)]
    return parts[0]


def reduce_all(x):
    axes = AXES
    sizes = [lax.axis_size(a) for a in axes]
    if any(s & (s - 1) for s in sizes):
        return lax.psum(x, axes)
    for axis, size in zip(axes, sizes):
        stride = 1
        while stride < size:
            radix = min(RADIX, size // stride)
            x = group_sum(x, axis, stride, radix)
            stride *= radix
    return x


def body(
    activations, cotangent, contig_lengths, gain_input, tap_weights, gain_middle, point_weights
):
    lengths = contig_lengths[0]
    shard_rows = activations.shape[1]
    seq_count = lax.axis_size("seq")
    tap_reach = SPAN * shard_rows
    total_length = shard_rows * seq_count
    tap_before = tap_weights[0]
    tap_center = tap_weights[1]
    tap_after = tap_weights[2]
    unit = shard_rows // sum(CHUNKS)
    first_row = lax.axis_index("seq") * shard_rows

    chunks = []
    start = 0
    for share in CHUNKS:
        rows = share * unit
        signal = activations[0, start:start + rows]
        upstream = cotangent[0, start:start + rows]
        positions = first_row + start + jnp.arange(rows, dtype=jnp.int32)
        start += rows
        owners = contig_owner(lengths, positions)
        before_valid = (
            (positions >= tap_reach) & (contig_owner(lengths, positions - tap_reach) == owners)
        ).astype(jnp.float32)[:, None]
        after_valid = (
            (positions < total_length - tap_reach)
            & (contig_owner(lengths, positions + tap_reach) == owners)
        ).astype(jnp.float32)[:, None]
        normed, input_vjp = jax.vjp(norm_activate, signal.astype(jnp.float32), gain_input)
        hidden = lax.optimization_barrier(normed.astype(jnp.bfloat16))
        sent_before = jnp.dot(hidden, tap_before, preferred_element_type=jnp.float32)
        sent_after = jnp.dot(hidden, tap_after, preferred_element_type=jnp.float32)
        chunks.append(dict(
            signal=signal, upstream=upstream, before_valid=before_valid,
            after_valid=after_valid, hidden=hidden, input_vjp=input_vjp,
            product_before=shifted(sent_before.astype(jnp.bfloat16), "seq", SPAN),
            product_after=shifted(sent_after.astype(jnp.bfloat16), "seq", -SPAN),
        ))
    for ch in chunks:
        combined = jnp.dot(ch["hidden"], tap_center, preferred_element_type=jnp.float32)
        grad_middle = jnp.dot(ch["upstream"], point_weights.T, preferred_element_type=jnp.float32)
        if EARLY:
            combined, grad_middle = lax.optimization_barrier((combined, grad_middle))
        combined = combined + ch["before_valid"] * ch["product_before"].astype(jnp.float32)
        combined = combined + ch["after_valid"] * ch["product_after"].astype(jnp.float32)
        middle_f, middle_vjp = jax.vjp(norm_activate, combined, gain_middle)
        ch["middle"] = middle_f.astype(jnp.bfloat16)
        grad_combined_f, ch["middle_terms"] = middle_vjp(grad_middle)
        grad_combined = grad_combined_f.astype(jnp.bfloat16)
        ch["grad_combined"] = grad_combined
        ch["combined_before"] = shifted(grad_combined, "seq", SPAN)
        ch["combined_after"] = shifted(grad_combined, "seq", -SPAN)
    if LATE_OUTPUT:
        last = chunks[-1]
        middles = [ch["middle"] for ch in chunks]
        middles, last["combined_before"], last["combined_after"] = lax.optimization_barrier(
            (middles, last["combined_before"], last["combined_after"])
        )
        for ch, middle in zip(chunks, middles):
            ch["middle"] = middle
    outputs, grads = [], []
    input_terms, middle_terms = None, None
    for ch in chunks:
        outputs.append((
            ch["signal"].astype(jnp.float32)
            + jnp.dot(ch["middle"], point_weights, preferred_element_type=jnp.float32)
        ).astype(jnp.bfloat16))
        grad_hidden = jnp.dot(ch["grad_combined"], tap_center.T, preferred_element_type=jnp.float32)
        grad_hidden = grad_hidden + ch["before_valid"] * jnp.dot(
            ch["combined_before"], tap_after.T, preferred_element_type=jnp.float32
        )
        grad_hidden = grad_hidden + ch["after_valid"] * jnp.dot(
            ch["combined_after"], tap_before.T, preferred_element_type=jnp.float32
        )
        grad_signal, terms = ch["input_vjp"](grad_hidden)
        grads.append((ch["upstream"].astype(jnp.float32) + grad_signal).astype(jnp.bfloat16))
        input_terms = terms if input_terms is None else input_terms + terms
        middle_terms = ch["middle_terms"] if middle_terms is None else middle_terms + ch["middle_terms"]
    summed = reduce_all(jnp.concatenate([input_terms, middle_terms]))
    factor = 1.0 / math.sqrt(lax.axis_size("batch") * seq_count * shard_rows)
    channels = input_terms.shape[0]
    return (
        jnp.concatenate(outputs)[None],
        jnp.concatenate(grads)[None],
        summed[:channels] * factor,
        summed[channels:] * factor,
    )


def solution(mesh):
    placed = (
        P("batch", "seq", None),
        P("batch", "seq", None),
        P("batch", None),
        P(),
        P(),
        P(),
        P(),
    )
    return jax.shard_map(
        body,
        mesh=mesh,
        in_specs=placed,
        out_specs=(P("batch", "seq", None), P("batch", "seq", None), P(), P()),
        check_vma=False,
    )
```

```python
import math

import jax
import jax.numpy as jnp
from jax import lax
from jax.sharding import PartitionSpec as P

SPAN = 2
CHUNKS = (1, 1)
AXES = ("seq", "batch")
STAGES = (2, 4, 4)
EARLY = True
LATE_OUTPUT = True


epsilon = 1e-06


def shifted(x, axis, by):
    peers = lax.axis_size(axis)
    pairs = [(i, i + by) for i in range(peers) if 0 <= i + by < peers]
    return lax.ppermute(x, axis, pairs)


def norm_activate(values, scales):
    mean_square = jnp.mean(values * values, axis=-1, keepdims=True)
    return jax.nn.gelu(values * lax.rsqrt(mean_square + epsilon) * scales, approximate=True)


def contig_owner(lengths, positions):
    bounds = jnp.cumsum(lengths)
    return jnp.sum((positions[:, None] >= bounds[None, :]).astype(jnp.int32), axis=1)


def group_sum(x, axis, stride, radix):
    size = lax.axis_size(axis)
    parts = [x]
    for step in range(1, radix):
        pairs = [(i, i ^ (step * stride)) for i in range(size)]
        parts.append(lax.ppermute(x, axis, pairs))
    while len(parts) > 1:
        parts = [parts[k] + parts[k + 1] for k in range(0, len(parts), 2)]
    return parts[0]


def reduce_all(x):
    axes = ("seq", "batch")
    size = lax.axis_size(axes)
    if size & (size - 1):
        return lax.psum(x, axes)
    stride = 1
    for radix in STAGES:
        if stride >= size:
            break
        radix = min(radix, size // stride)
        x = group_sum(x, axes, stride, radix)
        stride *= radix
    while stride < size:
        radix = min(4, size // stride)
        x = group_sum(x, axes, stride, radix)
        stride *= radix
    return x


def body(
    activations, cotangent, contig_lengths, gain_input, tap_weights, gain_middle, point_weights
):
    lengths = contig_lengths[0]
    shard_rows = activations.shape[1]
    seq_count = lax.axis_size("seq")
    tap_reach = SPAN * shard_rows
    total_length = shard_rows * seq_count
    tap_before = tap_weights[0]
    tap_center = tap_weights[1]
    tap_after = tap_weights[2]
    unit = shard_rows // sum(CHUNKS)
    first_row = lax.axis_index("seq") * shard_rows

    chunks = []
    start = 0
    for share in CHUNKS:
        rows = share * unit
        signal = activations[0, start:start + rows]
        upstream = cotangent[0, start:start + rows]
        positions = first_row + start + jnp.arange(rows, dtype=jnp.int32)
        start += rows
        owners = contig_owner(lengths, positions)
        before_valid = (
            (positions >= tap_reach) & (contig_owner(lengths, positions - tap_reach) == owners)
        ).astype(jnp.float32)[:, None]
        after_valid = (
            (positions < total_length - tap_reach)
            & (contig_owner(lengths, positions + tap_reach) == owners)
        ).astype(jnp.float32)[:, None]
        normed, input_vjp = jax.vjp(norm_activate, signal.astype(jnp.float32), gain_input)
        hidden = lax.optimization_barrier(normed.astype(jnp.bfloat16))
        sent_before = jnp.dot(hidden, tap_before, preferred_element_type=jnp.float32)
        sent_after = jnp.dot(hidden, tap_after, preferred_element_type=jnp.float32)
        chunks.append(dict(
            signal=signal, upstream=upstream, before_valid=before_valid,
            after_valid=after_valid, hidden=hidden, input_vjp=input_vjp,
            product_before=shifted(sent_before.astype(jnp.bfloat16), "seq", SPAN),
            product_after=shifted(sent_after.astype(jnp.bfloat16), "seq", -SPAN),
        ))
    for ch in chunks:
        combined = jnp.dot(ch["hidden"], tap_center, preferred_element_type=jnp.float32)
        grad_middle = jnp.dot(ch["upstream"], point_weights.T, preferred_element_type=jnp.float32)
        if EARLY:
            combined, grad_middle = lax.optimization_barrier((combined, grad_middle))
        combined = combined + ch["before_valid"] * ch["product_before"].astype(jnp.float32)
        combined = combined + ch["after_valid"] * ch["product_after"].astype(jnp.float32)
        middle_f, middle_vjp = jax.vjp(norm_activate, combined, gain_middle)
        ch["middle"] = middle_f.astype(jnp.bfloat16)
        grad_combined_f, ch["middle_terms"] = middle_vjp(grad_middle)
        grad_combined = grad_combined_f.astype(jnp.bfloat16)
        ch["grad_combined"] = grad_combined
        ch["combined_before"] = shifted(grad_combined, "seq", SPAN)
        ch["combined_after"] = shifted(grad_combined, "seq", -SPAN)
    if LATE_OUTPUT:
        last = chunks[-1]
        middles = [ch["middle"] for ch in chunks]
        middles, last["combined_before"], last["combined_after"] = lax.optimization_barrier(
            (middles, last["combined_before"], last["combined_after"])
        )
        for ch, middle in zip(chunks, middles):
            ch["middle"] = middle
    outputs, grads = [], []
    input_terms, middle_terms = None, None
    for ch in chunks:
        outputs.append((
            ch["signal"].astype(jnp.float32)
            + jnp.dot(ch["middle"], point_weights, preferred_element_type=jnp.float32)
        ).astype(jnp.bfloat16))
        grad_hidden = jnp.dot(ch["grad_combined"], tap_center.T, preferred_element_type=jnp.float32)
        grad_hidden = grad_hidden + ch["before_valid"] * jnp.dot(
            ch["combined_before"], tap_after.T, preferred_element_type=jnp.float32
        )
        grad_hidden = grad_hidden + ch["after_valid"] * jnp.dot(
            ch["combined_after"], tap_before.T, preferred_element_type=jnp.float32
        )
        grad_signal, terms = ch["input_vjp"](grad_hidden)
        grads.append((ch["upstream"].astype(jnp.float32) + grad_signal).astype(jnp.bfloat16))
        input_terms = terms if input_terms is None else input_terms + terms
        middle_terms = ch["middle_terms"] if middle_terms is None else middle_terms + ch["middle_terms"]
    summed = reduce_all(jnp.concatenate([input_terms, middle_terms]))
    factor = 1.0 / math.sqrt(lax.axis_size("batch") * seq_count * shard_rows)
    channels = input_terms.shape[0]
    return (
        jnp.concatenate(outputs)[None],
        jnp.concatenate(grads)[None],
        summed[:channels] * factor,
        summed[channels:] * factor,
    )


def solution(mesh):
    placed = (
        P("batch", "seq", None),
        P("batch", "seq", None),
        P("batch", None),
        P(),
        P(),
        P(),
        P(),
    )
    return jax.shard_map(
        body,
        mesh=mesh,
        in_specs=placed,
        out_specs=(P("batch", "seq", None), P("batch", "seq", None), P(), P()),
        check_vma=False,
    )
```

```python
import math

import jax
import jax.numpy as jnp
from jax import lax
from jax.sharding import PartitionSpec as P

SPAN = 2
CHUNKS = (1, 1)
AXES = ("seq", "batch")
STAGES = (2, 4, 4)
EARLY = True
LATE_OUTPUT = True


epsilon = 1e-06


def shifted(x, axis, by):
    peers = lax.axis_size(axis)
    pairs = [(i, i + by) for i in range(peers) if 0 <= i + by < peers]
    return lax.ppermute(x, axis, pairs)


def norm_activate(values, scales):
    mean_square = jnp.mean(values * values, axis=-1, keepdims=True)
    return jax.nn.gelu(values * lax.rsqrt(mean_square + epsilon) * scales, approximate=True)


def contig_owner(lengths, positions):
    bounds = jnp.cumsum(lengths)
    return jnp.sum((positions[:, None] >= bounds[None, :]).astype(jnp.int32), axis=1)


def group_sum(x, axis, stride, radix):
    size = lax.axis_size(axis)
    parts = [x]
    for step in range(1, radix):
        pairs = [(i, i ^ (step * stride)) for i in range(size)]
        parts.append(lax.ppermute(x, axis, pairs))
    while len(parts) > 1:
        parts = [parts[k] + parts[k + 1] for k in range(0, len(parts), 2)]
    return parts[0]


def reduce_all(x):
    axes = ("seq", "batch")
    size = lax.axis_size(axes)
    if size & (size - 1):
        return lax.psum(x, axes)
    stride, stages = 1, []
    for radix in STAGES:
        if stride < size:
            radix = min(radix, size // stride)
            stages.append((stride, radix))
            stride *= radix
    while stride < size:
        radix = min(4, size // stride)
        stages.append((stride, radix))
        stride *= radix
    for stride, radix in reversed(stages):
        x = group_sum(x, axes, stride, radix)
    return x


def body(
    activations, cotangent, contig_lengths, gain_input, tap_weights, gain_middle, point_weights
):
    lengths = contig_lengths[0]
    shard_rows = activations.shape[1]
    seq_count = lax.axis_size("seq")
    tap_reach = SPAN * shard_rows
    total_length = shard_rows * seq_count
    tap_before = tap_weights[0]
    tap_center = tap_weights[1]
    tap_after = tap_weights[2]
    unit = shard_rows // sum(CHUNKS)
    first_row = lax.axis_index("seq") * shard_rows

    chunks = []
    start = 0
    for share in CHUNKS:
        rows = share * unit
        signal = activations[0, start:start + rows]
        upstream = cotangent[0, start:start + rows]
        positions = first_row + start + jnp.arange(rows, dtype=jnp.int32)
        start += rows
        owners = contig_owner(lengths, positions)
        before_valid = (
            (positions >= tap_reach) & (contig_owner(lengths, positions - tap_reach) == owners)
        ).astype(jnp.float32)[:, None]
        after_valid = (
            (positions < total_length - tap_reach)
            & (contig_owner(lengths, positions + tap_reach) == owners)
        ).astype(jnp.float32)[:, None]
        normed, input_vjp = jax.vjp(norm_activate, signal.astype(jnp.float32), gain_input)
        hidden = lax.optimization_barrier(normed.astype(jnp.bfloat16))
        sent_before = jnp.dot(hidden, tap_before, preferred_element_type=jnp.float32)
        sent_after = jnp.dot(hidden, tap_after, preferred_element_type=jnp.float32)
        chunks.append(dict(
            signal=signal, upstream=upstream, before_valid=before_valid,
            after_valid=after_valid, hidden=hidden, input_vjp=input_vjp,
            product_before=shifted(sent_before.astype(jnp.bfloat16), "seq", SPAN),
            product_after=shifted(sent_after.astype(jnp.bfloat16), "seq", -SPAN),
        ))
    for ch in chunks:
        combined = jnp.dot(ch["hidden"], tap_center, preferred_element_type=jnp.float32)
        grad_middle = jnp.dot(ch["upstream"], point_weights.T, preferred_element_type=jnp.float32)
        if EARLY:
            combined, grad_middle = lax.optimization_barrier((combined, grad_middle))
        combined = combined + ch["before_valid"] * ch["product_before"].astype(jnp.float32)
        combined = combined + ch["after_valid"] * ch["product_after"].astype(jnp.float32)
        middle_f, middle_vjp = jax.vjp(norm_activate, combined, gain_middle)
        ch["middle"] = middle_f.astype(jnp.bfloat16)
        grad_combined_f, ch["middle_terms"] = middle_vjp(grad_middle)
        grad_combined = grad_combined_f.astype(jnp.bfloat16)
        ch["grad_combined"] = grad_combined
        ch["combined_before"] = shifted(grad_combined, "seq", SPAN)
        ch["combined_after"] = shifted(grad_combined, "seq", -SPAN)
    if LATE_OUTPUT:
        last = chunks[-1]
        middles = [ch["middle"] for ch in chunks]
        middles, last["combined_before"], last["combined_after"] = lax.optimization_barrier(
            (middles, last["combined_before"], last["combined_after"])
        )
        for ch, middle in zip(chunks, middles):
            ch["middle"] = middle
    outputs, grads = [], []
    input_terms, middle_terms = None, None
    for ch in chunks:
        outputs.append((
            ch["signal"].astype(jnp.float32)
            + jnp.dot(ch["middle"], point_weights, preferred_element_type=jnp.float32)
        ).astype(jnp.bfloat16))
        grad_hidden = jnp.dot(ch["grad_combined"], tap_center.T, preferred_element_type=jnp.float32)
        grad_hidden = grad_hidden + ch["before_valid"] * jnp.dot(
            ch["combined_before"], tap_after.T, preferred_element_type=jnp.float32
        )
        grad_hidden = grad_hidden + ch["after_valid"] * jnp.dot(
            ch["combined_after"], tap_before.T, preferred_element_type=jnp.float32
        )
        grad_signal, terms = ch["input_vjp"](grad_hidden)
        grads.append((ch["upstream"].astype(jnp.float32) + grad_signal).astype(jnp.bfloat16))
        input_terms = terms if input_terms is None else input_terms + terms
        middle_terms = ch["middle_terms"] if middle_terms is None else middle_terms + ch["middle_terms"]
    summed = reduce_all(jnp.concatenate([input_terms, middle_terms]))
    factor = 1.0 / math.sqrt(lax.axis_size("batch") * seq_count * shard_rows)
    channels = input_terms.shape[0]
    return (
        jnp.concatenate(outputs)[None],
        jnp.concatenate(grads)[None],
        summed[:channels] * factor,
        summed[channels:] * factor,
    )


def solution(mesh):
    placed = (
        P("batch", "seq", None),
        P("batch", "seq", None),
        P("batch", None),
        P(),
        P(),
        P(),
        P(),
    )
    return jax.shard_map(
        body,
        mesh=mesh,
        in_specs=placed,
        out_specs=(P("batch", "seq", None), P("batch", "seq", None), P(), P()),
        check_vma=False,
    )
```

```python
import math

import jax
import jax.numpy as jnp
from jax import lax
from jax.sharding import PartitionSpec as P

SPAN = 2
CHUNKS = (1, 1)
AXES = ("seq", "batch")
STAGES = (2, 4, 2, 2)
EARLY = True
LATE_OUTPUT = True


epsilon = 1e-06


def shifted(x, axis, by):
    peers = lax.axis_size(axis)
    pairs = [(i, i + by) for i in range(peers) if 0 <= i + by < peers]
    return lax.ppermute(x, axis, pairs)


def norm_activate(values, scales):
    mean_square = jnp.mean(values * values, axis=-1, keepdims=True)
    return jax.nn.gelu(values * lax.rsqrt(mean_square + epsilon) * scales, approximate=True)


def contig_owner(lengths, positions):
    bounds = jnp.cumsum(lengths)
    return jnp.sum((positions[:, None] >= bounds[None, :]).astype(jnp.int32), axis=1)


def group_sum(x, axis, stride, radix):
    size = lax.axis_size(axis)
    parts = [x]
    for step in range(1, radix):
        pairs = [(i, i ^ (step * stride)) for i in range(size)]
        parts.append(lax.ppermute(x, axis, pairs))
    while len(parts) > 1:
        parts = [parts[k] + parts[k + 1] for k in range(0, len(parts), 2)]
    return parts[0]


def reduce_all(x):
    axes = ("seq", "batch")
    size = lax.axis_size(axes)
    if size & (size - 1):
        return lax.psum(x, axes)
    stride, stages = 1, []
    for radix in STAGES:
        if stride < size:
            radix = min(radix, size // stride)
            stages.append((stride, radix))
            stride *= radix
    while stride < size:
        radix = min(4, size // stride)
        stages.append((stride, radix))
        stride *= radix
    for stride, radix in reversed(stages):
        x = group_sum(x, axes, stride, radix)
    return x


def body(
    activations, cotangent, contig_lengths, gain_input, tap_weights, gain_middle, point_weights
):
    lengths = contig_lengths[0]
    shard_rows = activations.shape[1]
    seq_count = lax.axis_size("seq")
    tap_reach = SPAN * shard_rows
    total_length = shard_rows * seq_count
    tap_before = tap_weights[0]
    tap_center = tap_weights[1]
    tap_after = tap_weights[2]
    unit = shard_rows // sum(CHUNKS)
    first_row = lax.axis_index("seq") * shard_rows

    chunks = []
    start = 0
    for share in CHUNKS:
        rows = share * unit
        signal = activations[0, start:start + rows]
        upstream = cotangent[0, start:start + rows]
        positions = first_row + start + jnp.arange(rows, dtype=jnp.int32)
        start += rows
        owners = contig_owner(lengths, positions)
        before_valid = (
            (positions >= tap_reach) & (contig_owner(lengths, positions - tap_reach) == owners)
        ).astype(jnp.float32)[:, None]
        after_valid = (
            (positions < total_length - tap_reach)
            & (contig_owner(lengths, positions + tap_reach) == owners)
        ).astype(jnp.float32)[:, None]
        normed, input_vjp = jax.vjp(norm_activate, signal.astype(jnp.float32), gain_input)
        hidden = lax.optimization_barrier(normed.astype(jnp.bfloat16))
        sent_before = jnp.dot(hidden, tap_before, preferred_element_type=jnp.float32)
        sent_after = jnp.dot(hidden, tap_after, preferred_element_type=jnp.float32)
        chunks.append(dict(
            signal=signal, upstream=upstream, before_valid=before_valid,
            after_valid=after_valid, hidden=hidden, input_vjp=input_vjp,
            product_before=shifted(sent_before.astype(jnp.bfloat16), "seq", SPAN),
            product_after=shifted(sent_after.astype(jnp.bfloat16), "seq", -SPAN),
        ))
    for ch in chunks:
        combined = jnp.dot(ch["hidden"], tap_center, preferred_element_type=jnp.float32)
        grad_middle = jnp.dot(ch["upstream"], point_weights.T, preferred_element_type=jnp.float32)
        if EARLY:
            combined, grad_middle = lax.optimization_barrier((combined, grad_middle))
        combined = combined + ch["before_valid"] * ch["product_before"].astype(jnp.float32)
        combined = combined + ch["after_valid"] * ch["product_after"].astype(jnp.float32)
        middle_f, middle_vjp = jax.vjp(norm_activate, combined, gain_middle)
        ch["middle"] = middle_f.astype(jnp.bfloat16)
        grad_combined_f, ch["middle_terms"] = middle_vjp(grad_middle)
        grad_combined = grad_combined_f.astype(jnp.bfloat16)
        ch["grad_combined"] = grad_combined
        ch["combined_before"] = shifted(grad_combined, "seq", SPAN)
        ch["combined_after"] = shifted(grad_combined, "seq", -SPAN)
    if LATE_OUTPUT:
        last = chunks[-1]
        middles = [ch["middle"] for ch in chunks]
        middles, last["combined_before"], last["combined_after"] = lax.optimization_barrier(
            (middles, last["combined_before"], last["combined_after"])
        )
        for ch, middle in zip(chunks, middles):
            ch["middle"] = middle
    outputs, grads = [], []
    input_terms, middle_terms = None, None
    for ch in chunks:
        outputs.append((
            ch["signal"].astype(jnp.float32)
            + jnp.dot(ch["middle"], point_weights, preferred_element_type=jnp.float32)
        ).astype(jnp.bfloat16))
        grad_hidden = jnp.dot(ch["grad_combined"], tap_center.T, preferred_element_type=jnp.float32)
        grad_hidden = grad_hidden + ch["before_valid"] * jnp.dot(
            ch["combined_before"], tap_after.T, preferred_element_type=jnp.float32
        )
        grad_hidden = grad_hidden + ch["after_valid"] * jnp.dot(
            ch["combined_after"], tap_before.T, preferred_element_type=jnp.float32
        )
        grad_signal, terms = ch["input_vjp"](grad_hidden)
        grads.append((ch["upstream"].astype(jnp.float32) + grad_signal).astype(jnp.bfloat16))
        input_terms = terms if input_terms is None else input_terms + terms
        middle_terms = ch["middle_terms"] if middle_terms is None else middle_terms + ch["middle_terms"]
    summed = reduce_all(jnp.concatenate([input_terms, middle_terms]))
    factor = 1.0 / math.sqrt(lax.axis_size("batch") * seq_count * shard_rows)
    channels = input_terms.shape[0]
    return (
        jnp.concatenate(outputs)[None],
        jnp.concatenate(grads)[None],
        summed[:channels] * factor,
        summed[channels:] * factor,
    )


def solution(mesh):
    placed = (
        P("batch", "seq", None),
        P("batch", "seq", None),
        P("batch", None),
        P(),
        P(),
        P(),
        P(),
    )
    return jax.shard_map(
        body,
        mesh=mesh,
        in_specs=placed,
        out_specs=(P("batch", "seq", None), P("batch", "seq", None), P(), P()),
        check_vma=False,
    )
```

```python
import math

import jax
import jax.numpy as jnp
from jax import lax
from jax.experimental import pallas as pl
from jax.sharding import PartitionSpec as P

SPAN = 2
CHUNKS = (1, 1)
AXES = ("seq", "batch")
STAGES = (2, 4, 2, 2)
EARLY = True
LATE_OUTPUT = True
BLOCK = 128


epsilon = 1e-06


def shifted(x, axis, by):
    peers = lax.axis_size(axis)
    pairs = [(i, i + by) for i in range(peers) if 0 <= i + by < peers]
    return lax.ppermute(x, axis, pairs)


def norm_activate(values, scales):
    mean_square = jnp.mean(values * values, axis=-1, keepdims=True)
    return jax.nn.gelu(values * lax.rsqrt(mean_square + epsilon) * scales, approximate=True)


def middle_kernel(center_ref, before_ref, after_ref, bv_ref, av_ref, grad_ref, gain_ref,
                  middle_ref, gc_ref, terms_ref):
    values = (center_ref[...] + bv_ref[...] * before_ref[...].astype(jnp.float32)
              + av_ref[...] * after_ref[...].astype(jnp.float32))
    width = values.shape[-1]
    scale = lax.rsqrt(jnp.sum(values * values, axis=-1, keepdims=True) / width + epsilon)
    gain = gain_ref[...]
    unit = values * scale
    z = unit * gain
    k = math.sqrt(2.0 / math.pi)
    t = jnp.tanh(k * (z + 0.044715 * z * z * z))
    middle_ref[...] = (0.5 * z * (1.0 + t)).astype(middle_ref.dtype)
    slope = 0.5 * (1.0 + t) + 0.5 * z * (1.0 - t * t) * k * (1.0 + 3.0 * 0.044715 * z * z)
    gz = grad_ref[...] * slope
    terms = jnp.sum(gz * unit, axis=0, keepdims=True)
    terms_ref[...] = jnp.broadcast_to(terms, terms_ref.shape)
    through = gz * gain
    inner = jnp.sum(through * values, axis=-1, keepdims=True)
    gc_ref[...] = (scale * through - values * (scale * scale * scale / width * inner)).astype(gc_ref.dtype)


def middle_block(center, before, after, bv, av, grad, gain):
    rows, width = center.shape
    blocks = rows // BLOCK
    row = pl.BlockSpec((BLOCK, width), lambda i: (i, 0))
    col = pl.BlockSpec((BLOCK, 1), lambda i: (i, 0))
    middle, gc, terms = pl.pallas_call(
        middle_kernel,
        grid=(blocks,),
        in_specs=[row, row, row, col, col, row, pl.BlockSpec((1, width), lambda i: (0, 0))],
        out_specs=[row, row, pl.BlockSpec((8, width), lambda i: (i, 0))],
        out_shape=[
            jax.ShapeDtypeStruct((rows, width), jnp.bfloat16),
            jax.ShapeDtypeStruct((rows, width), jnp.bfloat16),
            jax.ShapeDtypeStruct((blocks * 8, width), jnp.float32),
        ],
    )(center, before, after, bv, av, grad, gain.reshape(1, width))
    return middle, gc, jnp.sum(terms.reshape(blocks, 8, width)[:, 0], axis=0)


def contig_owner(lengths, positions):
    bounds = jnp.cumsum(lengths)
    return jnp.sum((positions[:, None] >= bounds[None, :]).astype(jnp.int32), axis=1)


def group_sum(x, axis, stride, radix):
    size = lax.axis_size(axis)
    parts = [x]
    for step in range(1, radix):
        pairs = [(i, i ^ (step * stride)) for i in range(size)]
        parts.append(lax.ppermute(x, axis, pairs))
    while len(parts) > 1:
        parts = [parts[k] + parts[k + 1] for k in range(0, len(parts), 2)]
    return parts[0]


def reduce_all(x):
    axes = ("seq", "batch")
    size = lax.axis_size(axes)
    if size & (size - 1):
        return lax.psum(x, axes)
    stride, stages = 1, []
    for radix in STAGES:
        if stride < size:
            radix = min(radix, size // stride)
            stages.append((stride, radix))
            stride *= radix
    while stride < size:
        radix = min(4, size // stride)
        stages.append((stride, radix))
        stride *= radix
    for stride, radix in reversed(stages):
        x = group_sum(x, axes, stride, radix)
    return x


def body(
    activations, cotangent, contig_lengths, gain_input, tap_weights, gain_middle, point_weights
):
    lengths = contig_lengths[0]
    shard_rows = activations.shape[1]
    seq_count = lax.axis_size("seq")
    tap_reach = SPAN * shard_rows
    total_length = shard_rows * seq_count
    tap_before = tap_weights[0]
    tap_center = tap_weights[1]
    tap_after = tap_weights[2]
    unit = shard_rows // sum(CHUNKS)
    first_row = lax.axis_index("seq") * shard_rows

    chunks = []
    start = 0
    for share in CHUNKS:
        rows = share * unit
        signal = activations[0, start:start + rows]
        upstream = cotangent[0, start:start + rows]
        positions = first_row + start + jnp.arange(rows, dtype=jnp.int32)
        start += rows
        owners = contig_owner(lengths, positions)
        before_valid = (
            (positions >= tap_reach) & (contig_owner(lengths, positions - tap_reach) == owners)
        ).astype(jnp.float32)[:, None]
        after_valid = (
            (positions < total_length - tap_reach)
            & (contig_owner(lengths, positions + tap_reach) == owners)
        ).astype(jnp.float32)[:, None]
        normed, input_vjp = jax.vjp(norm_activate, signal.astype(jnp.float32), gain_input)
        hidden = lax.optimization_barrier(normed.astype(jnp.bfloat16))
        sent_before = jnp.dot(hidden, tap_before, preferred_element_type=jnp.float32)
        sent_after = jnp.dot(hidden, tap_after, preferred_element_type=jnp.float32)
        chunks.append(dict(
            signal=signal, upstream=upstream, before_valid=before_valid,
            after_valid=after_valid, hidden=hidden, input_vjp=input_vjp,
            product_before=shifted(sent_before.astype(jnp.bfloat16), "seq", SPAN),
            product_after=shifted(sent_after.astype(jnp.bfloat16), "seq", -SPAN),
        ))
    for ch in chunks:
        combined = jnp.dot(ch["hidden"], tap_center, preferred_element_type=jnp.float32)
        grad_middle = jnp.dot(ch["upstream"], point_weights.T, preferred_element_type=jnp.float32)
        if EARLY:
            combined, grad_middle = lax.optimization_barrier((combined, grad_middle))
        ch["middle"], grad_combined, ch["middle_terms"] = middle_block(
            combined, ch["product_before"], ch["product_after"], ch["before_valid"],
            ch["after_valid"], grad_middle, gain_middle,
        )
        ch["grad_combined"] = grad_combined
        ch["combined_before"] = shifted(grad_combined, "seq", SPAN)
        ch["combined_after"] = shifted(grad_combined, "seq", -SPAN)
    if LATE_OUTPUT:
        last = chunks[-1]
        middles = [ch["middle"] for ch in chunks]
        middles, last["combined_before"], last["combined_after"] = lax.optimization_barrier(
            (middles, last["combined_before"], last["combined_after"])
        )
        for ch, middle in zip(chunks, middles):
            ch["middle"] = middle
    outputs, grads = [], []
    input_terms, middle_terms = None, None
    for ch in chunks:
        outputs.append((
            ch["signal"].astype(jnp.float32)
            + jnp.dot(ch["middle"], point_weights, preferred_element_type=jnp.float32)
        ).astype(jnp.bfloat16))
        grad_hidden = jnp.dot(ch["grad_combined"], tap_center.T, preferred_element_type=jnp.float32)
        grad_hidden = grad_hidden + ch["before_valid"] * jnp.dot(
            ch["combined_before"], tap_after.T, preferred_element_type=jnp.float32
        )
        grad_hidden = grad_hidden + ch["after_valid"] * jnp.dot(
            ch["combined_after"], tap_before.T, preferred_element_type=jnp.float32
        )
        grad_signal, terms = ch["input_vjp"](grad_hidden)
        grads.append((ch["upstream"].astype(jnp.float32) + grad_signal).astype(jnp.bfloat16))
        input_terms = terms if input_terms is None else input_terms + terms
        middle_terms = ch["middle_terms"] if middle_terms is None else middle_terms + ch["middle_terms"]
    summed = reduce_all(jnp.concatenate([input_terms, middle_terms]))
    factor = 1.0 / math.sqrt(lax.axis_size("batch") * seq_count * shard_rows)
    channels = input_terms.shape[0]
    return (
        jnp.concatenate(outputs)[None],
        jnp.concatenate(grads)[None],
        summed[:channels] * factor,
        summed[channels:] * factor,
    )


def solution(mesh):
    placed = (
        P("batch", "seq", None),
        P("batch", "seq", None),
        P("batch", None),
        P(),
        P(),
        P(),
        P(),
    )
    return jax.shard_map(
        body,
        mesh=mesh,
        in_specs=placed,
        out_specs=(P("batch", "seq", None), P("batch", "seq", None), P(), P()),
        check_vma=False,
    )
```
